512 devices in a mesh: dp: 32 (over z_lo, y, core), loop: 16 (over z_hi, x).
Axes of the slice: x: 4, y: 8, z: 8 (z_hi: 4, z_lo: 2; z = z_hi * 2 + z_lo), core: 2. Of those that a mesh axis runs over, the one named last changes fastest.
Arguments:
- tokens: bfloat16 [768, 3072], P('dp', 'loop'), may hold values from -6 to 6
- expert_ids: int32 [768, 2], P('dp'), may hold values from 0 to 7, all different within a row; in each aligned block of 24 rows (0 to 23, 24 to 47, ...) at most 10 rows name the same one
- route_logits: float32 [768, 2], P('dp'), may hold values from -8 to 8
- gate_weight: bfloat16 [32, 3072, 4096], P('dp', None, 'loop'), may hold values from -0.109375 to 0.109375
- up_weight: bfloat16 [32, 3072, 4096], P('dp', None, 'loop'), may hold values from -0.109375 to 0.109375
- down_weight: bfloat16 [32, 4096, 3072], P('dp', 'loop'), may hold values from -0.046875 to 0.046875
Outputs:
- mixed: bfloat16 [768, 3072], P('dp', 'loop')
The draws below stay inside these ranges and needn't reach their ends.
Inputs may be any that keep to these rules, and one draw needn't show every extreme that they name: `expert_ids`: the two experts of a token differ. Among the tokens of one index of dp (aligned blocks of 24 rows) no expert is named more than 10 times, a bound that some block reaches.
All inputs are finite; a program needn't handle non-finite values.
Results may differ from the reference program's by a relative error of at most 0.02.
Values may be sent and summed in bfloat16 or wider, within the bound.
No kernel may reach another device: no remote copies, remote signals or barrier semaphores. Data moves between devices by JAX's collectives and lax.ppermute only.
A program may use at most 64 MiB of HBM per device.

```python
import math
import jax
import jax.numpy as jnp
import numpy as np
from jax import lax

D = 3072
EXPERTS = 8
H_DEV = 256
TOK_DEV = 24
CAP = 10
FF = 16384
TOKENS = 768
N_DP = 32
N_LOOP = 16


def level_of(stream_key, dims, cuts, smallest, top_value):
    gain = 1.0
    for axis_at, shards_of in cuts:
        draws = jax.random.uniform(jax.random.fold_in(jax.random.fold_in(stream_key, 6), axis_at), (shards_of,), jnp.float32, smallest / len(cuts), top_value / len(cuts))
        gain = gain * jnp.repeat(jnp.exp(draws), dims[axis_at] // shards_of).reshape((-1,) + (1,) * (len(dims) - 1 - axis_at))
    return gain


def deal_out(own_key, own, number, rows, amount, top, reach, slope):
    ranking = jax.random.permutation(own_key, amount)
    heavy_load, ordinary = shares(amount, rows * top, reach, slope, True), shares(amount, rows * top, reach, slope, False)
    places = jnp.arange(amount)

    def named(lengths, offset_by):
        used = int((lengths > 0).sum())
        fixed = max(1, used // 4)
        moved = fixed + (places - fixed + offset_by * (used - fixed)) % max(1, amount - fixed)
        return jnp.zeros((amount,), jnp.int32).at[ranking[jnp.where(places < fixed, places, moved)]].set(jnp.asarray(lengths, jnp.int32))

    lengths = jnp.where(number % 4 == 0, named(heavy_load, number // 4), named(ordinary, number - number // 4 - 1))
    mixed = jax.random.permutation(jax.random.fold_in(own, 3), amount)
    donor, taker = mixed[0:amount // 2 * 2:2], mixed[1:amount // 2 * 2:2]
    margin = jnp.minimum(lengths[donor] - 1, reach - lengths[taker]) // 2
    margin = jnp.where((donor == ranking[0]) | (taker == ranking[0]) | (lengths[taker] == 0), 0, jnp.maximum(margin, 0))
    moved = jax.random.randint(jax.random.fold_in(own, 4), (amount // 2,), 0, 1 << 20) % (margin + 1)
    lengths = lengths.at[donor].add(-moved).at[taker].add(moved)
    members = jnp.searchsorted(jnp.cumsum(lengths), jnp.arange(rows * top), side="right").astype(jnp.int32)
    listing = members.reshape(top, rows).T
    listing = listing[jax.random.permutation(jax.random.fold_in(own, 1), rows)]
    offset_by = jax.random.randint(jax.random.fold_in(own, 2), (rows, 1), 0, top)
    return jnp.take_along_axis(listing, (jnp.arange(top)[None, :] + offset_by) % top, axis=1)


def shares(count, total, reach, slope, full):
    portions = [(1 << 20) // math.isqrt(standing ** slope) + 1 for standing in range(1, count + 1)]
    largest = reach if full else min(reach, max(-(-total // count), total * portions[0] // sum(portions)))
    least = 1 if total - largest >= count - 1 else 0
    given, surplus = [largest] + [least] * (count - 1), total - largest - least * (count - 1)
    while surplus > 0:
        free = [i for i in range(1, count) if given[i] < largest] or [i for i in range(1, count) if given[i] < reach]
        whole, left = sum([portions[i] for i in free]), surplus
        for i in free:
            extra = min(reach - given[i], max(1, left * portions[i] // whole), surplus)
            given[i] = given[i] + extra
            surplus = surplus - extra
    return np.array(given)


def normal_values(key, dims, spread, bound, cuts=(), kind=jnp.bfloat16):
    drawn = jax.random.normal(key, dims, jnp.float32) * spread
    if len(cuts) > 0:
        drawn = level_of(key, dims, cuts, -0.22, 0.18) * drawn
    return jnp.clip(drawn, min=-bound, max=bound).astype(kind)


def setup_inputs(seed: int = 0) -> dict:
    key_of = jax.random.split(jax.random.key(seed), 7)
    tokens = normal_values(key_of[0], (TOKENS, D), 1.0, 6.0, ((0, 32), (1, 16)))
    expert_ids_keys = jax.random.split(jax.random.fold_in(key_of[1], 1), TOKENS // TOK_DEV)
    expert_ids_turns = jax.random.permutation(jax.random.fold_in(key_of[1], 3), TOKENS // TOK_DEV)
    expert_ids = jax.vmap(lambda own, number: deal_out(jax.random.fold_in(key_of[1], 2), own, number, TOK_DEV, EXPERTS, 2, CAP, 2))(expert_ids_keys, expert_ids_turns).reshape((TOKENS, 2))
    route_logits = normal_values(key_of[2], (TOKENS, 2), 2.0, 8.0, ((0, 32),), jnp.float32)
    gate_weight = normal_values(key_of[3], (N_DP, D, H_DEV * N_LOOP), D ** -0.5, 0.109375, ((0, 32), (2, 16)))
    up_weight = normal_values(key_of[4], (N_DP, D, H_DEV * N_LOOP), D ** -0.5, 0.109375, ((0, 32), (2, 16)))
    down_weight = normal_values(key_of[5], (N_DP, H_DEV * N_LOOP, D), FF ** -0.5, 0.046875, ((0, 32), (1, 16)))
    return dict(tokens=tokens, expert_ids=expert_ids, route_logits=route_logits, gate_weight=gate_weight, up_weight=up_weight, down_weight=down_weight)


def reference(tokens, expert_ids, route_logits, gate_weight, up_weight, down_weight):
    copies = N_DP // EXPERTS
    assigned = expert_ids.reshape(N_DP, TOK_DEV * 2)
    onehot = (assigned[:, :, None] == jnp.arange(EXPERTS, dtype=jnp.int32)[None, None, :]).astype(jnp.int32)
    before = jnp.cumsum(onehot, axis=1) - onehot
    position = jnp.sum(before * onehot, axis=2)
    slot_index = jnp.arange(EXPERTS * CAP, dtype=jnp.int32)
    picker = (slot_index[None, :, None] == (assigned * CAP + position)[:, None, :]).astype(jnp.float32)
    picker = picker.reshape(N_DP, EXPERTS * CAP, TOK_DEV, 2).sum(axis=3)
    features = tokens.reshape(N_DP, TOK_DEV, D).astype(jnp.float32)
    buffers = jnp.einsum("sct,std->scd", picker, features).astype(jnp.bfloat16)
    buffers = buffers.reshape(N_DP, EXPERTS, CAP, D)

    def expert_slice(target):
        expert = target // copies
        buffer_rows = lax.dynamic_index_in_dim(buffers, expert, 1, keepdims=False).reshape(N_DP * CAP, D)
        gate_local = lax.dynamic_index_in_dim(gate_weight, target, 0, keepdims=False)
        up_local = lax.dynamic_index_in_dim(up_weight, target, 0, keepdims=False)
        down_local = lax.dynamic_index_in_dim(down_weight, target, 0, keepdims=False)
        gate_sum = jnp.dot(buffer_rows, gate_local, preferred_element_type=jnp.float32)
        up_sum = jnp.dot(buffer_rows, up_local, preferred_element_type=jnp.float32)
        hidden = (jax.nn.silu(gate_sum) * up_sum).astype(jnp.bfloat16)
        pieces = hidden.reshape(N_DP * CAP, N_LOOP, H_DEV).astype(jnp.float32)
        down_parts = down_local.reshape(N_LOOP, H_DEV, D).astype(jnp.float32)
        partials = jnp.einsum("rlh,lhd->lrd", pieces, down_parts).astype(jnp.bfloat16)
        return jnp.sum(partials.astype(jnp.float32), axis=0).astype(jnp.bfloat16)

    results = lax.map(expert_slice, jnp.arange(N_DP, dtype=jnp.int32))
    results = results.reshape(N_DP, N_DP, CAP, D).transpose(1, 0, 2, 3).reshape(N_DP, N_DP * CAP, D)
    column_index = jnp.arange(N_DP * CAP, dtype=jnp.int32)
    same_expert = ((column_index // CAP) // copies)[None, None, :] == assigned[:, :, None]
    same_slot = (column_index % CAP)[None, None, :] == position[:, :, None]
    collector = (same_expert & same_slot).astype(jnp.float32)
    gathered = jnp.einsum("sac,scd->sad", collector, results.astype(jnp.float32))
    gathered = gathered.reshape(TOKENS, 2, D)
    weights = jax.nn.sigmoid(route_logits - route_logits[:, ::-1])
    mixed = jnp.sum(weights[:, :, None] * gathered, axis=1)
    return mixed.astype(jnp.bfloat16)
```

```python
import jax
import jax.numpy as jnp
from jax import lax
from jax.sharding import Mesh
from jax.sharding import PartitionSpec as P

EXPERTS = 8
CAP = 10
GROUP_AXES = ("zl", "yh", "yl")
LOOP_AXES = ("zh", "x")


def assignment_slots(expert_ids):
    assigned = expert_ids.reshape(-1)
    onehot = (assigned[:, None] == jnp.arange(EXPERTS, dtype=jnp.int32)[None, :]).astype(jnp.int32)
    before = jnp.cumsum(onehot, axis=0) - onehot
    return (assigned, jnp.sum(before * onehot, axis=1))


def swap_cores(x):
    return lax.ppermute(x, "c", [(0, 1), (1, 0)])


def body(tokens, expert_ids, route_logits, gate_weight, up_weight, down_weight):
    peers = lax.axis_size(GROUP_AXES)
    n_loop = lax.axis_size(LOOP_AXES)
    halves = peers // EXPERTS
    tok_count, slice_width = tokens.shape
    model_width = gate_weight.shape[1]
    hidden_width = gate_weight.shape[2]
    rows = peers * CAP
    assigned, position = assignment_slots(expert_ids)
    slot_index = jnp.arange(EXPERTS * CAP, dtype=jnp.int32)
    picker = (slot_index[:, None] == (assigned * CAP + position)[None, :]).astype(jnp.bfloat16)
    picker = picker.reshape(EXPERTS * CAP, tok_count, 2).sum(axis=2)
    packed = jnp.dot(picker, tokens, preferred_element_type=jnp.float32).astype(jnp.bfloat16)
    packed = packed.reshape(EXPERTS, CAP, slice_width)
    arrived = lax.all_to_all(
        jnp.repeat(packed, halves, axis=0), GROUP_AXES, split_axis=0, concat_axis=0, tiled=True
    )
    lane = 128
    dense = arrived.reshape(rows * slice_width // lane, lane)
    spread = lax.all_to_all(
        jnp.broadcast_to(dense[None], (n_loop,) + dense.shape), LOOP_AXES, 0, 0, tiled=True
    )
    own = spread.reshape(n_loop, rows, slice_width)
    other = swap_cores(spread).reshape(n_loop, rows, slice_width)
    segment = jnp.concatenate([own, other], axis=1)
    segment = segment.transpose(1, 0, 2).reshape(2 * rows, model_width)
    gate_sum = jnp.dot(segment, gate_weight[0], preferred_element_type=jnp.float32)
    up_sum = jnp.dot(segment, up_weight[0], preferred_element_type=jnp.float32)
    hidden = (jax.nn.silu(gate_sum) * up_sum).astype(jnp.bfloat16)
    partial = jnp.dot(hidden, down_weight[0], preferred_element_type=jnp.float32)
    partner_part = swap_cores(partial[rows:].astype(jnp.bfloat16))
    pair_sum = (partial[:rows] + partner_part.astype(jnp.float32)).astype(jnp.bfloat16)
    by_slice = pair_sum.reshape(rows, n_loop, slice_width).transpose(1, 0, 2)
    by_slice = by_slice.reshape(n_loop, rows * slice_width // lane, lane)
    summed = lax.all_to_all(by_slice, LOOP_AXES, 0, 0, tiled=True)
    summed = summed.reshape(n_loop, rows, slice_width).astype(jnp.float32).sum(axis=0)
    expert_out = summed.astype(jnp.bfloat16).reshape(peers, CAP, slice_width)
    returned = lax.all_to_all(expert_out, GROUP_AXES, split_axis=0, concat_axis=0, tiled=True).reshape(
        rows, slice_width
    )
    column_index = jnp.arange(rows, dtype=jnp.int32)
    same_expert = (column_index // CAP // halves)[None, :] == assigned[:, None]
    same_slot = (column_index % CAP)[None, :] == position[:, None]
    collector = (same_expert & same_slot).astype(jnp.bfloat16)
    gathered = jnp.dot(collector, returned, preferred_element_type=jnp.float32).reshape(
        tok_count, 2, slice_width
    )
    weights = jax.nn.sigmoid(route_logits - route_logits[:, ::-1])
    mixed = jnp.sum(weights[:, :, None] * gathered, axis=1)
    return mixed.astype(jnp.bfloat16)


def solution(mesh):
    dp, loop = mesh.shape["dp"], mesh.shape["loop"]
    fine = Mesh(
        mesh.devices.reshape(2, dp // 8, 2, 2, loop // 4, 4), GROUP_AXES + ("c",) + LOOP_AXES
    )
    dp_axes = GROUP_AXES + ("c",)
    in_specs = (
        P(dp_axes, LOOP_AXES),
        P(dp_axes, None),
        P(dp_axes, None),
        P(dp_axes, None, LOOP_AXES),
        P(dp_axes, None, LOOP_AXES),
        P(dp_axes, LOOP_AXES, None),
    )
    out_specs = P(dp_axes, LOOP_AXES)
    return jax.shard_map(body, mesh=fine, in_specs=in_specs, out_specs=out_specs, check_vma=False)
```

```python
import jax
import jax.numpy as jnp
from jax import lax
from jax.sharding import Mesh
from jax.sharding import PartitionSpec as P

EXPERTS = 8
CAP = 10
GROUP_AXES = ("zl", "yh", "yl")
LOOP_AXES = ("zh", "x")


def assignment_slots(expert_ids):
    assigned = expert_ids.reshape(-1)
    onehot = (assigned[:, None] == jnp.arange(EXPERTS, dtype=jnp.int32)[None, :]).astype(jnp.int32)
    before = jnp.cumsum(onehot, axis=0) - onehot
    return (assigned, jnp.sum(before * onehot, axis=1))


def swap_cores(x):
    return lax.ppermute(x, "c", [(0, 1), (1, 0)])


def body(tokens, expert_ids, route_logits, gate_weight, up_weight, down_weight):
    peers = lax.axis_size(GROUP_AXES)
    n_loop = lax.axis_size(LOOP_AXES)
    halves = peers // EXPERTS
    tok_count, slice_width = tokens.shape
    model_width = gate_weight.shape[1]
    hidden_width = gate_weight.shape[2]
    rows = peers * CAP
    assigned, position = assignment_slots(expert_ids)
    slot_index = jnp.arange(EXPERTS * CAP, dtype=jnp.int32)
    picker = (slot_index[:, None] == (assigned * CAP + position)[None, :]).astype(jnp.bfloat16)
    picker = picker.reshape(EXPERTS * CAP, tok_count, 2).sum(axis=2)
    packed = jnp.dot(picker, tokens, preferred_element_type=jnp.float32).astype(jnp.bfloat16)
    packed = packed.reshape(EXPERTS, CAP, slice_width)
    arrived = lax.all_to_all(
        jnp.repeat(packed, halves, axis=0), GROUP_AXES, split_axis=0, concat_axis=0, tiled=True
    )
    spread = lax.all_to_all(
        jnp.broadcast_to(arrived.reshape(1, rows, slice_width), (n_loop, rows, slice_width)),
        LOOP_AXES, 0, 2, tiled=True,
    ).reshape(rows, model_width)
    segment = jnp.concatenate([spread, swap_cores(spread)], axis=0)
    gate_sum = jnp.dot(segment, gate_weight[0], preferred_element_type=jnp.float32)
    up_sum = jnp.dot(segment, up_weight[0], preferred_element_type=jnp.float32)
    hidden = (jax.nn.silu(gate_sum) * up_sum).astype(jnp.bfloat16)
    partial = jnp.dot(hidden, down_weight[0], preferred_element_type=jnp.float32)
    partner_part = swap_cores(partial[rows:].astype(jnp.bfloat16))
    pair_sum = (partial[:rows] + partner_part.astype(jnp.float32)).astype(jnp.bfloat16)
    summed = lax.all_to_all(pair_sum.reshape(1, rows, model_width), LOOP_AXES, 2, 0, tiled=True)
    summed = summed.astype(jnp.float32).sum(axis=0)
    expert_out = summed.astype(jnp.bfloat16).reshape(peers, CAP, slice_width)
    returned = lax.all_to_all(expert_out, GROUP_AXES, split_axis=0, concat_axis=0, tiled=True).reshape(
        rows, slice_width
    )
    column_index = jnp.arange(rows, dtype=jnp.int32)
    same_expert = (column_index // CAP // halves)[None, :] == assigned[:, None]
    same_slot = (column_index % CAP)[None, :] == position[:, None]
    collector = (same_expert & same_slot).astype(jnp.bfloat16)
    gathered = jnp.dot(collector, returned, preferred_element_type=jnp.float32).reshape(
        tok_count, 2, slice_width
    )
    weights = jax.nn.sigmoid(route_logits - route_logits[:, ::-1])
    mixed = jnp.sum(weights[:, :, None] * gathered, axis=1)
    return mixed.astype(jnp.bfloat16)


def solution(mesh):
    dp, loop = mesh.shape["dp"], mesh.shape["loop"]
    fine = Mesh(
        mesh.devices.reshape(2, dp // 8, 2, 2, loop // 4, 4), GROUP_AXES + ("c",) + LOOP_AXES
    )
    dp_axes = GROUP_AXES + ("c",)
    in_specs = (
        P(dp_axes, LOOP_AXES),
        P(dp_axes, None),
        P(dp_axes, None),
        P(dp_axes, None, LOOP_AXES),
        P(dp_axes, None, LOOP_AXES),
        P(dp_axes, LOOP_AXES, None),
    )
    out_specs = P(dp_axes, LOOP_AXES)
    return jax.shard_map(body, mesh=fine, in_specs=in_specs, out_specs=out_specs, check_vma=False)
```

```python
import jax
import jax.numpy as jnp
from jax import lax
from jax.sharding import Mesh
from jax.sharding import PartitionSpec as P

EXPERTS = 8
CAP = 10
GROUP_AXES = ("zl", "yh", "yl")
LOOP_AXES = ("zh", "x")


def assignment_slots(expert_ids):
    assigned = expert_ids.reshape(-1)
    onehot = (assigned[:, None] == jnp.arange(EXPERTS, dtype=jnp.int32)[None, :]).astype(jnp.int32)
    before = jnp.cumsum(onehot, axis=0) - onehot
    return (assigned, jnp.sum(before * onehot, axis=1))


def swap_cores(x):
    return lax.ppermute(x, "c", [(0, 1), (1, 0)])


def body(tokens, expert_ids, route_logits, gate_weight, up_weight, down_weight):
    peers = lax.axis_size(GROUP_AXES)
    n_loop = lax.axis_size(LOOP_AXES)
    halves = peers // EXPERTS
    tok_count, slice_width = tokens.shape
    model_width = gate_weight.shape[1]
    hidden_width = gate_weight.shape[2]
    rows = peers * CAP
    assigned, position = assignment_slots(expert_ids)
    slot_index = jnp.arange(EXPERTS * CAP, dtype=jnp.int32)
    picker = (slot_index[:, None] == (assigned * CAP + position)[None, :]).astype(jnp.bfloat16)
    picker = picker.reshape(EXPERTS * CAP, tok_count, 2).sum(axis=2)
    packed = jnp.dot(picker, tokens, preferred_element_type=jnp.float32).astype(jnp.bfloat16)
    packed = packed.reshape(EXPERTS, CAP, slice_width)
    arrived = lax.all_to_all(
        jnp.repeat(packed, halves, axis=0), GROUP_AXES, split_axis=0, concat_axis=0, tiled=True
    )
    lane = 128
    dense = arrived.reshape(rows * slice_width // lane, lane)
    spread = lax.all_to_all(
        jnp.broadcast_to(dense[None], (n_loop,) + dense.shape), LOOP_AXES, 0, 0, tiled=True
    )
    other = swap_cores(spread)
    segment = jnp.concatenate([spread, other], axis=1).reshape(n_loop, 2 * rows, slice_width)
    segment = segment.transpose(1, 0, 2).reshape(2 * rows, model_width)
    gate_sum = jnp.dot(segment, gate_weight[0], preferred_element_type=jnp.float32)
    up_sum = jnp.dot(segment, up_weight[0], preferred_element_type=jnp.float32)
    hidden = (jax.nn.silu(gate_sum) * up_sum).astype(jnp.bfloat16)
    down_t = (((0,), (1,)), ((), ()))
    own_t = lax.dot_general(down_weight[0], hidden[:rows], down_t, preferred_element_type=jnp.float32)
    other_t = lax.dot_general(down_weight[0], hidden[rows:], down_t, preferred_element_type=jnp.float32)
    partner_t = swap_cores(other_t.astype(jnp.bfloat16))
    pair_t = (own_t + partner_t.astype(jnp.float32)).astype(jnp.bfloat16)
    by_slice = pair_t.reshape(n_loop, slice_width * rows // lane, lane)
    summed = lax.all_to_all(by_slice, LOOP_AXES, 0, 0, tiled=True)
    summed = summed.astype(jnp.float32).sum(axis=0).reshape(slice_width, rows).T
    expert_out = summed.astype(jnp.bfloat16).reshape(peers, CAP, slice_width)
    returned = lax.all_to_all(expert_out, GROUP_AXES, split_axis=0, concat_axis=0, tiled=True).reshape(
        rows, slice_width
    )
    column_index = jnp.arange(rows, dtype=jnp.int32)
    same_expert = (column_index // CAP // halves)[None, :] == assigned[:, None]
    same_slot = (column_index % CAP)[None, :] == position[:, None]
    collector = (same_expert & same_slot).astype(jnp.bfloat16)
    gathered = jnp.dot(collector, returned, preferred_element_type=jnp.float32).reshape(
        tok_count, 2, slice_width
    )
    weights = jax.nn.sigmoid(route_logits - route_logits[:, ::-1])
    mixed = jnp.sum(weights[:, :, None] * gathered, axis=1)
    return mixed.astype(jnp.bfloat16)


def solution(mesh):
    dp, loop = mesh.shape["dp"], mesh.shape["loop"]
    fine = Mesh(
        mesh.devices.reshape(2, dp // 8, 2, 2, loop // 4, 4), GROUP_AXES + ("c",) + LOOP_AXES
    )
    dp_axes = GROUP_AXES + ("c",)
    in_specs = (
        P(dp_axes, LOOP_AXES),
        P(dp_axes, None),
        P(dp_axes, None),
        P(dp_axes, None, LOOP_AXES),
        P(dp_axes, None, LOOP_AXES),
        P(dp_axes, LOOP_AXES, None),
    )
    out_specs = P(dp_axes, LOOP_AXES)
    return jax.shard_map(body, mesh=fine, in_specs=in_specs, out_specs=out_specs, check_vma=False)
```

```python
import jax
import jax.numpy as jnp
from jax import lax
from jax.sharding import Mesh
from jax.sharding import PartitionSpec as P

EXPERTS = 8
CAP = 10
GROUP_AXES = ("zl", "yh", "yl")
LOOP_AXES = ("zh", "x")


def assignment_slots(expert_ids):
    assigned = expert_ids.reshape(-1)
    onehot = (assigned[:, None] == jnp.arange(EXPERTS, dtype=jnp.int32)[None, :]).astype(jnp.int32)
    before = jnp.cumsum(onehot, axis=0) - onehot
    return (assigned, jnp.sum(before * onehot, axis=1))


def swap_cores(x):
    return lax.ppermute(x, "c", [(0, 1), (1, 0)])


def body(tokens, expert_ids, route_logits, gate_weight, up_weight, down_weight):
    peers = lax.axis_size(GROUP_AXES)
    n_loop = lax.axis_size(LOOP_AXES)
    halves = peers // EXPERTS
    tok_count, slice_width = tokens.shape
    model_width = gate_weight.shape[1]
    hidden_width = gate_weight.shape[2]
    rows = peers * CAP
    assigned, position = assignment_slots(expert_ids)
    slot_index = jnp.arange(EXPERTS * CAP, dtype=jnp.int32)
    picker = (slot_index[:, None] == (assigned * CAP + position)[None, :]).astype(jnp.bfloat16)
    picker = picker.reshape(EXPERTS * CAP, tok_count, 2).sum(axis=2)
    packed = jnp.dot(picker, tokens, preferred_element_type=jnp.float32).astype(jnp.bfloat16)
    packed = packed.reshape(EXPERTS, CAP, slice_width)
    arrived = lax.all_to_all(
        jnp.repeat(packed, halves, axis=0), GROUP_AXES, split_axis=0, concat_axis=0, tiled=True
    )
    lane = 128
    dense = arrived.reshape(rows * slice_width // lane, lane)
    spread = lax.all_to_all(
        jnp.broadcast_to(dense[None], (n_loop,) + dense.shape), LOOP_AXES, 0, 0, tiled=True
    )
    other = swap_cores(spread)
    segment = jnp.concatenate([spread, other], axis=1).reshape(n_loop, 2 * rows, slice_width)
    by_block = (n_loop, slice_width, hidden_width)
    gate_sum = jnp.einsum(
        "lrf,lfh->rh", segment, gate_weight[0].reshape(by_block), preferred_element_type=jnp.float32
    )
    up_sum = jnp.einsum(
        "lrf,lfh->rh", segment, up_weight[0].reshape(by_block), preferred_element_type=jnp.float32
    )
    hidden = (jax.nn.silu(gate_sum) * up_sum).astype(jnp.bfloat16)
    down_t = (((0,), (1,)), ((), ()))
    own_t = lax.dot_general(down_weight[0], hidden[:rows], down_t, preferred_element_type=jnp.float32)
    other_t = lax.dot_general(down_weight[0], hidden[rows:], down_t, preferred_element_type=jnp.float32)
    partner_t = swap_cores(other_t.astype(jnp.bfloat16))
    pair_t = (own_t + partner_t.astype(jnp.float32)).astype(jnp.bfloat16)
    by_slice = pair_t.reshape(n_loop, slice_width * rows // lane, lane)
    summed = lax.all_to_all(by_slice, LOOP_AXES, 0, 0, tiled=True)
    summed = summed.astype(jnp.float32).sum(axis=0).reshape(slice_width, rows).T
    expert_out = summed.astype(jnp.bfloat16).reshape(peers, CAP, slice_width)
    returned = lax.all_to_all(expert_out, GROUP_AXES, split_axis=0, concat_axis=0, tiled=True).reshape(
        rows, slice_width
    )
    column_index = jnp.arange(rows, dtype=jnp.int32)
    same_expert = (column_index // CAP // halves)[None, :] == assigned[:, None]
    same_slot = (column_index % CAP)[None, :] == position[:, None]
    collector = (same_expert & same_slot).astype(jnp.bfloat16)
    gathered = jnp.dot(collector, returned, preferred_element_type=jnp.float32).reshape(
        tok_count, 2, slice_width
    )
    weights = jax.nn.sigmoid(route_logits - route_logits[:, ::-1])
    mixed = jnp.sum(weights[:, :, None] * gathered, axis=1)
    return mixed.astype(jnp.bfloat16)


def solution(mesh):
    dp, loop = mesh.shape["dp"], mesh.shape["loop"]
    fine = Mesh(
        mesh.devices.reshape(2, dp // 8, 2, 2, loop // 4, 4), GROUP_AXES + ("c",) + LOOP_AXES
    )
    dp_axes = GROUP_AXES + ("c",)
    in_specs = (
        P(dp_axes, LOOP_AXES),
        P(dp_axes, None),
        P(dp_axes, None),
        P(dp_axes, None, LOOP_AXES),
        P(dp_axes, None, LOOP_AXES),
        P(dp_axes, LOOP_AXES, None),
    )
    out_specs = P(dp_axes, LOOP_AXES)
    return jax.shard_map(body, mesh=fine, in_specs=in_specs, out_specs=out_specs, check_vma=False)
```

```python
import jax
import jax.numpy as jnp
from jax import lax
from jax.sharding import Mesh
from jax.sharding import PartitionSpec as P

EXPERTS = 8
CAP = 10
GROUP_AXES = ("zl", "yh", "yl")
LOOP_AXES = ("zh", "x")


def assignment_slots(expert_ids):
    assigned = expert_ids.reshape(-1)
    onehot = (assigned[:, None] == jnp.arange(EXPERTS, dtype=jnp.int32)[None, :]).astype(jnp.int32)
    before = jnp.cumsum(onehot, axis=0) - onehot
    return (assigned, jnp.sum(before * onehot, axis=1))


def swap_cores(x):
    return lax.ppermute(x, "c", [(0, 1), (1, 0)])


def body(tokens, expert_ids, route_logits, gate_weight, up_weight, down_weight):
    peers = lax.axis_size(GROUP_AXES)
    n_loop = lax.axis_size(LOOP_AXES)
    halves = peers // EXPERTS
    tok_count, slice_width = tokens.shape
    model_width = gate_weight.shape[1]
    hidden_width = gate_weight.shape[2]
    rows = peers * CAP
    assigned, position = assignment_slots(expert_ids)
    slot_index = jnp.arange(EXPERTS * CAP, dtype=jnp.int32)
    picker = (slot_index[:, None] == (assigned * CAP + position)[None, :]).astype(jnp.bfloat16)
    picker = picker.reshape(EXPERTS * CAP, tok_count, 2).sum(axis=2)
    packed = jnp.dot(picker, tokens, preferred_element_type=jnp.float32).astype(jnp.bfloat16)
    packed = packed.reshape(EXPERTS, CAP, slice_width)
    arrived = lax.all_to_all(
        jnp.repeat(packed, halves, axis=0), GROUP_AXES, split_axis=0, concat_axis=0, tiled=True
    )
    lane = 128
    dense = arrived.reshape(rows * slice_width // lane, lane)
    spread = lax.all_to_all(
        jnp.broadcast_to(dense[None], (n_loop,) + dense.shape), LOOP_AXES, 0, 0, tiled=True
    )
    other = swap_cores(spread)
    by_block = (n_loop, slice_width, hidden_width)
    gate_blocks = gate_weight[0].reshape(by_block)
    up_blocks = up_weight[0].reshape(by_block)
    down_t = (((0,), (1,)), ((), ()))

    def project(gathered):
        segment = gathered.reshape(n_loop, rows, slice_width)
        gate_sum = jnp.einsum("lrf,lfh->rh", segment, gate_blocks, preferred_element_type=jnp.float32)
        up_sum = jnp.einsum("lrf,lfh->rh", segment, up_blocks, preferred_element_type=jnp.float32)
        hidden = (jax.nn.silu(gate_sum) * up_sum).astype(jnp.bfloat16)
        return lax.dot_general(down_weight[0], hidden, down_t, preferred_element_type=jnp.float32)

    partner_t = swap_cores(project(other).astype(jnp.bfloat16))
    own_t = project(spread)
    pair_t = (own_t + partner_t.astype(jnp.float32)).astype(jnp.bfloat16)
    by_slice = pair_t.reshape(n_loop, slice_width * rows // lane, lane)
    summed = lax.all_to_all(by_slice, LOOP_AXES, 0, 0, tiled=True)
    summed = summed.astype(jnp.float32).sum(axis=0).reshape(slice_width, rows).T
    expert_out = summed.astype(jnp.bfloat16).reshape(peers, CAP, slice_width)
    returned = lax.all_to_all(expert_out, GROUP_AXES, split_axis=0, concat_axis=0, tiled=True).reshape(
        rows, slice_width
    )
    column_index = jnp.arange(rows, dtype=jnp.int32)
    same_expert = (column_index // CAP // halves)[None, :] == assigned[:, None]
    same_slot = (column_index % CAP)[None, :] == position[:, None]
    collector = (same_expert & same_slot).astype(jnp.bfloat16)
    gathered = jnp.dot(collector, returned, preferred_element_type=jnp.float32).reshape(
        tok_count, 2, slice_width
    )
    weights = jax.nn.sigmoid(route_logits - route_logits[:, ::-1])
    mixed = jnp.sum(weights[:, :, None] * gathered, axis=1)
    return mixed.astype(jnp.bfloat16)


def solution(mesh):
    dp, loop = mesh.shape["dp"], mesh.shape["loop"]
    fine = Mesh(
        mesh.devices.reshape(2, dp // 8, 2, 2, loop // 4, 4), GROUP_AXES + ("c",) + LOOP_AXES
    )
    dp_axes = GROUP_AXES + ("c",)
    in_specs = (
        P(dp_axes, LOOP_AXES),
        P(dp_axes, None),
        P(dp_axes, None),
        P(dp_axes, None, LOOP_AXES),
        P(dp_axes, None, LOOP_AXES),
        P(dp_axes, LOOP_AXES, None),
    )
    out_specs = P(dp_axes, LOOP_AXES)
    return jax.shard_map(body, mesh=fine, in_specs=in_specs, out_specs=out_specs, check_vma=False)
```

```python
import jax
import jax.numpy as jnp
from jax import lax
from jax.sharding import Mesh
from jax.sharding import PartitionSpec as P

EXPERTS = 8
CAP = 10
GROUP_AXES = ("zl", "yh", "yl")
LOOP_AXES = ("zh", "x")


def assignment_slots(expert_ids):
    assigned = expert_ids.reshape(-1)
    onehot = (assigned[:, None] == jnp.arange(EXPERTS, dtype=jnp.int32)[None, :]).astype(jnp.int32)
    before = jnp.cumsum(onehot, axis=0) - onehot
    return (assigned, jnp.sum(before * onehot, axis=1))


def swap_cores(x):
    return lax.ppermute(x, "c", [(0, 1), (1, 0)])


def body(tokens, expert_ids, route_logits, gate_weight, up_weight, down_weight):
    peers = lax.axis_size(GROUP_AXES)
    n_loop = lax.axis_size(LOOP_AXES)
    halves = peers // EXPERTS
    tok_count, slice_width = tokens.shape
    model_width = gate_weight.shape[1]
    hidden_width = gate_weight.shape[2]
    rows = peers * CAP
    assigned, position = assignment_slots(expert_ids)
    slot_index = jnp.arange(EXPERTS * CAP, dtype=jnp.int32)
    picker = (slot_index[:, None] == (assigned * CAP + position)[None, :]).astype(jnp.bfloat16)
    picker = picker.reshape(EXPERTS * CAP, tok_count, 2).sum(axis=2)
    packed = jnp.dot(picker, tokens, preferred_element_type=jnp.float32).astype(jnp.bfloat16)
    packed = packed.reshape(EXPERTS, CAP, slice_width)
    arrived = lax.all_to_all(
        jnp.repeat(packed, halves, axis=0), GROUP_AXES, split_axis=0, concat_axis=0, tiled=True
    )
    lane = 128
    dense = arrived.reshape(rows * slice_width // lane, lane)
    n_z, n_x = lax.axis_size(LOOP_AXES[0]), lax.axis_size(LOOP_AXES[1])
    planes = lax.all_to_all(
        jnp.broadcast_to(dense[None], (n_z,) + dense.shape), LOOP_AXES[0], 0, 0, tiled=True
    )
    spread = lax.all_to_all(
        jnp.broadcast_to(planes[None], (n_x,) + planes.shape), LOOP_AXES[1], 0, 0, tiled=True
    )
    other = swap_cores(spread)
    segment = jnp.concatenate([spread, other], axis=2).reshape(n_x, n_z, 2 * rows, slice_width)
    by_block = (n_z, n_x, slice_width, hidden_width)
    gate_sum = jnp.einsum(
        "xzrf,zxfh->rh", segment, gate_weight[0].reshape(by_block), preferred_element_type=jnp.float32
    )
    up_sum = jnp.einsum(
        "xzrf,zxfh->rh", segment, up_weight[0].reshape(by_block), preferred_element_type=jnp.float32
    )
    hidden = (jax.nn.silu(gate_sum) * up_sum).astype(jnp.bfloat16)
    down_t = (((0,), (1,)), ((), ()))
    own_t = lax.dot_general(down_weight[0], hidden[:rows], down_t, preferred_element_type=jnp.float32)
    other_t = lax.dot_general(down_weight[0], hidden[rows:], down_t, preferred_element_type=jnp.float32)
    partner_t = swap_cores(other_t.astype(jnp.bfloat16))
    pair_t = (own_t + partner_t.astype(jnp.float32)).astype(jnp.bfloat16)
    by_slice = pair_t.reshape(n_loop, slice_width * rows // lane, lane)
    summed = lax.all_to_all(by_slice, LOOP_AXES, 0, 0, tiled=True)
    summed = summed.astype(jnp.float32).sum(axis=0).reshape(slice_width, rows).T
    expert_out = summed.astype(jnp.bfloat16).reshape(peers, CAP, slice_width)
    returned = lax.all_to_all(expert_out, GROUP_AXES, split_axis=0, concat_axis=0, tiled=True).reshape(
        rows, slice_width
    )
    column_index = jnp.arange(rows, dtype=jnp.int32)
    same_expert = (column_index // CAP // halves)[None, :] == assigned[:, None]
    same_slot = (column_index % CAP)[None, :] == position[:, None]
    collector = (same_expert & same_slot).astype(jnp.bfloat16)
    gathered = jnp.dot(collector, returned, preferred_element_type=jnp.float32).reshape(
        tok_count, 2, slice_width
    )
    weights = jax.nn.sigmoid(route_logits - route_logits[:, ::-1])
    mixed = jnp.sum(weights[:, :, None] * gathered, axis=1)
    return mixed.astype(jnp.bfloat16)


def solution(mesh):
    dp, loop = mesh.shape["dp"], mesh.shape["loop"]
    fine = Mesh(
        mesh.devices.reshape(2, dp // 8, 2, 2, loop // 4, 4), GROUP_AXES + ("c",) + LOOP_AXES
    )
    dp_axes = GROUP_AXES + ("c",)
    in_specs = (
        P(dp_axes, LOOP_AXES),
        P(dp_axes, None),
        P(dp_axes, None),
        P(dp_axes, None, LOOP_AXES),
        P(dp_axes, None, LOOP_AXES),
        P(dp_axes, LOOP_AXES, None),
    )
    out_specs = P(dp_axes, LOOP_AXES)
    return jax.shard_map(body, mesh=fine, in_specs=in_specs, out_specs=out_specs, check_vma=False)
```

```python
import jax
import jax.numpy as jnp
from jax import lax
from jax.sharding import Mesh
from jax.sharding import PartitionSpec as P

EXPERTS = 8
CAP = 10
GROUP_AXES = ("zl", "yh", "yl")
LOOP_AXES = ("zh", "x")


def assignment_slots(expert_ids):
    assigned = expert_ids.reshape(-1)
    onehot = (assigned[:, None] == jnp.arange(EXPERTS, dtype=jnp.int32)[None, :]).astype(jnp.int32)
    before = jnp.cumsum(onehot, axis=0) - onehot
    return (assigned, jnp.sum(before * onehot, axis=1))


def swap_cores(x):
    return lax.ppermute(x, "c", [(0, 1), (1, 0)])


def body(tokens, expert_ids, route_logits, gate_weight, up_weight, down_weight):
    peers = lax.axis_size(GROUP_AXES)
    n_loop = lax.axis_size(LOOP_AXES)
    halves = peers // EXPERTS
    tok_count, slice_width = tokens.shape
    model_width = gate_weight.shape[1]
    hidden_width = gate_weight.shape[2]
    rows = peers * CAP
    assigned, position = assignment_slots(expert_ids)
    slot_index = jnp.arange(EXPERTS * CAP, dtype=jnp.int32)
    picker = (slot_index[:, None] == (assigned * CAP + position)[None, :]).astype(jnp.bfloat16)
    picker = picker.reshape(EXPERTS * CAP, tok_count, 2).sum(axis=2)
    packed = jnp.dot(picker, tokens, preferred_element_type=jnp.float32).astype(jnp.bfloat16)
    packed = packed.reshape(EXPERTS, CAP, slice_width)
    arrived = lax.all_to_all(
        jnp.repeat(packed, halves, axis=0), GROUP_AXES, split_axis=0, concat_axis=0, tiled=True
    )
    lane = 128
    dense = arrived.reshape(rows * slice_width // lane, lane)
    n_z, n_x = lax.axis_size(LOOP_AXES[0]), lax.axis_size(LOOP_AXES[1])
    planes = lax.all_to_all(
        jnp.broadcast_to(dense[None], (n_z,) + dense.shape), LOOP_AXES[0], 0, 0, tiled=True
    )
    spread = lax.all_to_all(
        jnp.broadcast_to(planes[None], (n_x,) + planes.shape), LOOP_AXES[1], 0, 0, tiled=True
    )
    other = swap_cores(spread)
    segment = jnp.concatenate([spread, other], axis=2).reshape(n_x, n_z, 2 * rows, slice_width)
    by_block = (n_z, n_x, slice_width, hidden_width)
    gate_sum = jnp.einsum(
        "xzrf,zxfh->rh", segment, gate_weight[0].reshape(by_block), preferred_element_type=jnp.float32
    )
    up_sum = jnp.einsum(
        "xzrf,zxfh->rh", segment, up_weight[0].reshape(by_block), preferred_element_type=jnp.float32
    )
    hidden = (jax.nn.silu(gate_sum) * up_sum).astype(jnp.bfloat16)
    down_t = (((0,), (1,)), ((), ()))
    own_t = lax.dot_general(down_weight[0], hidden[:rows], down_t, preferred_element_type=jnp.float32)
    other_t = lax.dot_general(down_weight[0], hidden[rows:], down_t, preferred_element_type=jnp.float32)
    partner_t = swap_cores(other_t.astype(jnp.bfloat16))
    pair_t = (own_t + partner_t.astype(jnp.float32)).astype(jnp.bfloat16)
    by_slice = pair_t.reshape(n_z, n_x, slice_width * rows // lane, lane)
    x_sum = lax.all_to_all(by_slice, LOOP_AXES[1], 1, 1, tiled=True)
    x_sum = x_sum.astype(jnp.float32).sum(axis=1).astype(jnp.bfloat16)
    summed = lax.all_to_all(x_sum, LOOP_AXES[0], 0, 0, tiled=True)
    summed = summed.astype(jnp.float32).sum(axis=0).reshape(slice_width, rows).T
    expert_out = summed.astype(jnp.bfloat16).reshape(peers, CAP, slice_width)
    returned = lax.all_to_all(expert_out, GROUP_AXES, split_axis=0, concat_axis=0, tiled=True).reshape(
        rows, slice_width
    )
    column_index = jnp.arange(rows, dtype=jnp.int32)
    same_expert = (column_index // CAP // halves)[None, :] == assigned[:, None]
    same_slot = (column_index % CAP)[None, :] == position[:, None]
    collector = (same_expert & same_slot).astype(jnp.bfloat16)
    gathered = jnp.dot(collector, returned, preferred_element_type=jnp.float32).reshape(
        tok_count, 2, slice_width
    )
    weights = jax.nn.sigmoid(route_logits - route_logits[:, ::-1])
    mixed = jnp.sum(weights[:, :, None] * gathered, axis=1)
    return mixed.astype(jnp.bfloat16)


def solution(mesh):
    dp, loop = mesh.shape["dp"], mesh.shape["loop"]
    fine = Mesh(
        mesh.devices.reshape(2, dp // 8, 2, 2, loop // 4, 4), GROUP_AXES + ("c",) + LOOP_AXES
    )
    dp_axes = GROUP_AXES + ("c",)
    in_specs = (
        P(dp_axes, LOOP_AXES),
        P(dp_axes, None),
        P(dp_axes, None),
        P(dp_axes, None, LOOP_AXES),
        P(dp_axes, None, LOOP_AXES),
        P(dp_axes, LOOP_AXES, None),
    )
    out_specs = P(dp_axes, LOOP_AXES)
    return jax.shard_map(body, mesh=fine, in_specs=in_specs, out_specs=out_specs, check_vma=False)
```

```python
import jax
import jax.numpy as jnp
from jax import lax
from jax.sharding import Mesh
from jax.sharding import PartitionSpec as P

EXPERTS = 8
CAP = 10
GROUP_AXES = ("zl", "yh", "yl")
LOOP_AXES = ("zh", "x")


def assignment_slots(expert_ids):
    assigned = expert_ids.reshape(-1)
    onehot = (assigned[:, None] == jnp.arange(EXPERTS, dtype=jnp.int32)[None, :]).astype(jnp.int32)
    before = jnp.cumsum(onehot, axis=0) - onehot
    return (assigned, jnp.sum(before * onehot, axis=1))


def swap_cores(x):
    return lax.ppermute(x, "c", [(0, 1), (1, 0)])


def body(tokens, expert_ids, route_logits, gate_weight, up_weight, down_weight):
    peers = lax.axis_size(GROUP_AXES)
    n_loop = lax.axis_size(LOOP_AXES)
    halves = peers // EXPERTS
    tok_count, slice_width = tokens.shape
    model_width = gate_weight.shape[1]
    hidden_width = gate_weight.shape[2]
    rows = peers * CAP
    assigned, position = assignment_slots(expert_ids)
    slot_index = jnp.arange(EXPERTS * CAP, dtype=jnp.int32)
    picker = (slot_index[:, None] == (assigned * CAP + position)[None, :]).astype(jnp.bfloat16)
    picker = picker.reshape(EXPERTS * CAP, tok_count, 2).sum(axis=2)
    n_z, n_x = lax.axis_size(LOOP_AXES[0]), lax.axis_size(LOOP_AXES[1])
    plane_tokens = lax.all_to_all(
        jnp.broadcast_to(tokens[None], (n_z,) + tokens.shape), LOOP_AXES[0], 0, 0, tiled=True
    )
    packed = jnp.einsum("st,ztf->szf", picker, plane_tokens, preferred_element_type=jnp.float32)
    packed = packed.astype(jnp.bfloat16).reshape(EXPERTS, CAP, n_z * slice_width)
    arrived = lax.all_to_all(
        jnp.repeat(packed, halves, axis=0), GROUP_AXES, split_axis=0, concat_axis=0, tiled=True
    ).reshape(rows, n_z * slice_width)
    spread = lax.all_to_all(
        jnp.broadcast_to(arrived[None], (n_x,) + arrived.shape), LOOP_AXES[1], 0, 0, tiled=True
    )
    other = swap_cores(spread)
    segment = jnp.concatenate([spread, other], axis=1).reshape(n_x, 2 * rows, n_z, slice_width)
    by_block = (n_z, n_x, slice_width, hidden_width)
    gate_sum = jnp.einsum(
        "xrzf,zxfh->rh", segment, gate_weight[0].reshape(by_block), preferred_element_type=jnp.float32
    )
    up_sum = jnp.einsum(
        "xrzf,zxfh->rh", segment, up_weight[0].reshape(by_block), preferred_element_type=jnp.float32
    )
    hidden = (jax.nn.silu(gate_sum) * up_sum).astype(jnp.bfloat16)
    down_t = (((0,), (1,)), ((), ()))
    own_t = lax.dot_general(down_weight[0], hidden[:rows], down_t, preferred_element_type=jnp.float32)
    other_t = lax.dot_general(down_weight[0], hidden[rows:], down_t, preferred_element_type=jnp.float32)
    partner_t = swap_cores(other_t.astype(jnp.bfloat16))
    pair_t = (own_t + partner_t.astype(jnp.float32)).astype(jnp.bfloat16)
    lane = 128
    by_slice = pair_t.reshape(n_loop, slice_width * rows // lane, lane)
    summed = lax.all_to_all(by_slice, LOOP_AXES, 0, 0, tiled=True)
    summed = summed.astype(jnp.float32).sum(axis=0).reshape(slice_width, rows).T
    expert_out = summed.astype(jnp.bfloat16).reshape(peers, CAP, slice_width)
    returned = lax.all_to_all(expert_out, GROUP_AXES, split_axis=0, concat_axis=0, tiled=True).reshape(
        rows, slice_width
    )
    column_index = jnp.arange(rows, dtype=jnp.int32)
    same_expert = (column_index // CAP // halves)[None, :] == assigned[:, None]
    same_slot = (column_index % CAP)[None, :] == position[:, None]
    collector = (same_expert & same_slot).astype(jnp.bfloat16)
    gathered = jnp.dot(collector, returned, preferred_element_type=jnp.float32).reshape(
        tok_count, 2, slice_width
    )
    weights = jax.nn.sigmoid(route_logits - route_logits[:, ::-1])
    mixed = jnp.sum(weights[:, :, None] * gathered, axis=1)
    return mixed.astype(jnp.bfloat16)


def solution(mesh):
    dp, loop = mesh.shape["dp"], mesh.shape["loop"]
    fine = Mesh(
        mesh.devices.reshape(2, dp // 8, 2, 2, loop // 4, 4), GROUP_AXES + ("c",) + LOOP_AXES
    )
    dp_axes = GROUP_AXES + ("c",)
    in_specs = (
        P(dp_axes, LOOP_AXES),
        P(dp_axes, None),
        P(dp_axes, None),
        P(dp_axes, None, LOOP_AXES),
        P(dp_axes, None, LOOP_AXES),
        P(dp_axes, LOOP_AXES, None),
    )
    out_specs = P(dp_axes, LOOP_AXES)
    return jax.shard_map(body, mesh=fine, in_specs=in_specs, out_specs=out_specs, check_vma=False)
```

```python
import jax
import jax.numpy as jnp
from jax import lax
from jax.sharding import Mesh
from jax.sharding import PartitionSpec as P

EXPERTS = 8
CAP = 10
GROUP_AXES = ("zl", "yh", "yl")
LOOP_AXES = ("zh", "x")


def assignment_slots(expert_ids):
    assigned = expert_ids.reshape(-1)
    onehot = (assigned[:, None] == jnp.arange(EXPERTS, dtype=jnp.int32)[None, :]).astype(jnp.int32)
    before = jnp.cumsum(onehot, axis=0) - onehot
    return (assigned, jnp.sum(before * onehot, axis=1))


def swap_cores(x):
    return lax.ppermute(x, "c", [(0, 1), (1, 0)])


def body(tokens, expert_ids, route_logits, gate_weight, up_weight, down_weight):
    peers = lax.axis_size(GROUP_AXES)
    n_loop = lax.axis_size(LOOP_AXES)
    halves = peers // EXPERTS
    tok_count, slice_width = tokens.shape
    model_width = gate_weight.shape[1]
    hidden_width = gate_weight.shape[2]
    rows = peers * CAP
    assigned, position = assignment_slots(expert_ids)
    slot_index = jnp.arange(EXPERTS * CAP, dtype=jnp.int32)
    picker = (slot_index[:, None] == (assigned * CAP + position)[None, :]).astype(jnp.bfloat16)
    picker = picker.reshape(EXPERTS * CAP, tok_count, 2).sum(axis=2)
    packed = jnp.dot(picker, tokens, preferred_element_type=jnp.float32).astype(jnp.bfloat16)
    packed = packed.reshape(EXPERTS, CAP, slice_width)
    n_z, n_x = lax.axis_size(LOOP_AXES[0]), lax.axis_size(LOOP_AXES[1])
    outgoing = jnp.broadcast_to(
        jnp.repeat(packed, halves, axis=0)[:, None], (peers, n_z, CAP, slice_width)
    ).reshape(peers * n_z, CAP, slice_width)
    arrived = lax.all_to_all(
        outgoing, GROUP_AXES + LOOP_AXES[:1], split_axis=0, concat_axis=0, tiled=True
    ).reshape(peers, n_z, CAP, slice_width)
    lane = 128
    planes = arrived.transpose(1, 0, 2, 3).reshape(n_z, rows * slice_width // lane, lane)
    spread = lax.all_to_all(
        jnp.broadcast_to(planes[None], (n_x,) + planes.shape), LOOP_AXES[1], 0, 0, tiled=True
    )
    other = swap_cores(spread)
    segment = jnp.concatenate([spread, other], axis=2).reshape(n_x, n_z, 2 * rows, slice_width)
    by_block = (n_z, n_x, slice_width, hidden_width)
    gate_sum = jnp.einsum(
        "xzrf,zxfh->rh", segment, gate_weight[0].reshape(by_block), preferred_element_type=jnp.float32
    )
    up_sum = jnp.einsum(
        "xzrf,zxfh->rh", segment, up_weight[0].reshape(by_block), preferred_element_type=jnp.float32
    )
    hidden = (jax.nn.silu(gate_sum) * up_sum).astype(jnp.bfloat16)
    down_t = (((0,), (1,)), ((), ()))
    own_t = lax.dot_general(down_weight[0], hidden[:rows], down_t, preferred_element_type=jnp.float32)
    other_t = lax.dot_general(down_weight[0], hidden[rows:], down_t, preferred_element_type=jnp.float32)
    partner_t = swap_cores(other_t.astype(jnp.bfloat16))
    pair_t = (own_t + partner_t.astype(jnp.float32)).astype(jnp.bfloat16)
    by_slice = pair_t.reshape(n_loop, slice_width * rows // lane, lane)
    summed = lax.all_to_all(by_slice, LOOP_AXES, 0, 0, tiled=True)
    summed = summed.astype(jnp.float32).sum(axis=0).reshape(slice_width, rows).T
    expert_out = summed.astype(jnp.bfloat16).reshape(peers, CAP, slice_width)
    returned = lax.all_to_all(expert_out, GROUP_AXES, split_axis=0, concat_axis=0, tiled=True).reshape(
        rows, slice_width
    )
    column_index = jnp.arange(rows, dtype=jnp.int32)
    same_expert = (column_index // CAP // halves)[None, :] == assigned[:, None]
    same_slot = (column_index % CAP)[None, :] == position[:, None]
    collector = (same_expert & same_slot).astype(jnp.bfloat16)
    gathered = jnp.dot(collector, returned, preferred_element_type=jnp.float32).reshape(
        tok_count, 2, slice_width
    )
    weights = jax.nn.sigmoid(route_logits - route_logits[:, ::-1])
    mixed = jnp.sum(weights[:, :, None] * gathered, axis=1)
    return mixed.astype(jnp.bfloat16)


def solution(mesh):
    dp, loop = mesh.shape["dp"], mesh.shape["loop"]
    fine = Mesh(
        mesh.devices.reshape(2, dp // 8, 2, 2, loop // 4, 4), GROUP_AXES + ("c",) + LOOP_AXES
    )
    dp_axes = GROUP_AXES + ("c",)
    in_specs = (
        P(dp_axes, LOOP_AXES),
        P(dp_axes, None),
        P(dp_axes, None),
        P(dp_axes, None, LOOP_AXES),
        P(dp_axes, None, LOOP_AXES),
        P(dp_axes, LOOP_AXES, None),
    )
    out_specs = P(dp_axes, LOOP_AXES)
    return jax.shard_map(body, mesh=fine, in_specs=in_specs, out_specs=out_specs, check_vma=False)
```

```python
import jax
import jax.numpy as jnp
from jax import lax
from jax.sharding import Mesh
from jax.sharding import PartitionSpec as P

EXPERTS = 8
CAP = 10
GROUP_AXES = ("zl", "yh", "yl")
LOOP_AXES = ("zh", "x")


def assignment_slots(expert_ids):
    assigned = expert_ids.reshape(-1)
    onehot = (assigned[:, None] == jnp.arange(EXPERTS, dtype=jnp.int32)[None, :]).astype(jnp.int32)
    before = jnp.cumsum(onehot, axis=0) - onehot
    return (assigned, jnp.sum(before * onehot, axis=1))


def swap_cores(x):
    return lax.ppermute(x, "c", [(0, 1), (1, 0)])


def body(tokens, expert_ids, route_logits, gate_weight, up_weight, down_weight):
    peers = lax.axis_size(GROUP_AXES)
    n_loop = lax.axis_size(LOOP_AXES)
    halves = peers // EXPERTS
    tok_count, slice_width = tokens.shape
    model_width = gate_weight.shape[1]
    hidden_width = gate_weight.shape[2]
    rows = peers * CAP
    assigned, position = assignment_slots(expert_ids)
    slot_index = jnp.arange(EXPERTS * CAP, dtype=jnp.int32)
    picker = (slot_index[:, None] == (assigned * CAP + position)[None, :]).astype(jnp.bfloat16)
    picker = picker.reshape(EXPERTS * CAP, tok_count, 2).sum(axis=2)
    packed = jnp.dot(picker, tokens, preferred_element_type=jnp.float32).astype(jnp.bfloat16)
    packed = packed.reshape(EXPERTS, CAP, slice_width)
    n_z, n_x = lax.axis_size(LOOP_AXES[0]), lax.axis_size(LOOP_AXES[1])
    outgoing = jnp.broadcast_to(
        jnp.repeat(packed, halves, axis=0)[:, None], (peers, n_z, CAP, slice_width)
    ).reshape(peers * n_z, CAP, slice_width)
    arrived = lax.all_to_all(
        outgoing, GROUP_AXES + LOOP_AXES[:1], split_axis=0, concat_axis=0, tiled=True
    ).reshape(peers, n_z, CAP, slice_width)
    lane = 128
    planes = arrived.transpose(1, 0, 2, 3).reshape(n_z, rows * slice_width // lane, lane)
    spread = lax.all_to_all(
        jnp.broadcast_to(planes[None], (n_x,) + planes.shape), LOOP_AXES[1], 0, 0, tiled=True
    )
    other = swap_cores(spread)
    segment = jnp.concatenate([spread, other], axis=2).reshape(n_x, n_z, 2 * rows, slice_width)
    by_block = (n_z, n_x, slice_width, hidden_width)
    gate_sum = jnp.einsum(
        "xzrf,zxfh->rh", segment, gate_weight[0].reshape(by_block), preferred_element_type=jnp.float32
    )
    up_sum = jnp.einsum(
        "xzrf,zxfh->rh", segment, up_weight[0].reshape(by_block), preferred_element_type=jnp.float32
    )
    hidden = (jax.nn.silu(gate_sum) * up_sum).astype(jnp.bfloat16)
    down_t = (((0,), (1,)), ((), ()))
    own_t = lax.dot_general(down_weight[0], hidden[:rows], down_t, preferred_element_type=jnp.float32)
    other_t = lax.dot_general(down_weight[0], hidden[rows:], down_t, preferred_element_type=jnp.float32)
    partner_t = swap_cores(other_t.astype(jnp.bfloat16))
    pair_t = (own_t + partner_t.astype(jnp.float32)).astype(jnp.bfloat16)
    by_slice = pair_t.reshape(n_z, n_x, slice_width * rows // lane, lane)
    x_sum = lax.all_to_all(by_slice, LOOP_AXES[1], 1, 1, tiled=True)
    x_sum = x_sum.astype(jnp.float32).sum(axis=1).astype(jnp.bfloat16)
    x_sum = x_sum.reshape(n_z, slice_width, peers, CAP).transpose(2, 0, 3, 1)
    back = lax.all_to_all(
        x_sum.reshape(peers * n_z, CAP, slice_width), GROUP_AXES + LOOP_AXES[:1], 0, 0, tiled=True
    )
    returned = back.reshape(peers, n_z, CAP, slice_width).astype(jnp.float32).sum(axis=1)
    returned = returned.astype(jnp.bfloat16).reshape(rows, slice_width)
    column_index = jnp.arange(rows, dtype=jnp.int32)
    same_expert = (column_index // CAP // halves)[None, :] == assigned[:, None]
    same_slot = (column_index % CAP)[None, :] == position[:, None]
    collector = (same_expert & same_slot).astype(jnp.bfloat16)
    gathered = jnp.dot(collector, returned, preferred_element_type=jnp.float32).reshape(
        tok_count, 2, slice_width
    )
    weights = jax.nn.sigmoid(route_logits - route_logits[:, ::-1])
    mixed = jnp.sum(weights[:, :, None] * gathered, axis=1)
    return mixed.astype(jnp.bfloat16)


def solution(mesh):
    dp, loop = mesh.shape["dp"], mesh.shape["loop"]
    fine = Mesh(
        mesh.devices.reshape(2, dp // 8, 2, 2, loop // 4, 4), GROUP_AXES + ("c",) + LOOP_AXES
    )
    dp_axes = GROUP_AXES + ("c",)
    in_specs = (
        P(dp_axes, LOOP_AXES),
        P(dp_axes, None),
        P(dp_axes, None),
        P(dp_axes, None, LOOP_AXES),
        P(dp_axes, None, LOOP_AXES),
        P(dp_axes, LOOP_AXES, None),
    )
    out_specs = P(dp_axes, LOOP_AXES)
    return jax.shard_map(body, mesh=fine, in_specs=in_specs, out_specs=out_specs, check_vma=False)
```

```python
import jax
import jax.numpy as jnp
from jax import lax
from jax.sharding import Mesh
from jax.sharding import PartitionSpec as P

EXPERTS = 8
CAP = 10
GROUP_AXES = ("zl", "yh", "yl")
LOOP_AXES = ("zh", "x")


def assignment_slots(expert_ids):
    assigned = expert_ids.reshape(-1)
    onehot = (assigned[:, None] == jnp.arange(EXPERTS, dtype=jnp.int32)[None, :]).astype(jnp.int32)
    before = jnp.cumsum(onehot, axis=0) - onehot
    return (assigned, jnp.sum(before * onehot, axis=1))


def swap_cores(x):
    return lax.ppermute(x, "c", [(0, 1), (1, 0)])


def body(tokens, expert_ids, route_logits, gate_weight, up_weight, down_weight):
    peers = lax.axis_size(GROUP_AXES)
    n_loop = lax.axis_size(LOOP_AXES)
    halves = peers // EXPERTS
    tok_count, slice_width = tokens.shape
    model_width = gate_weight.shape[1]
    hidden_width = gate_weight.shape[2]
    rows = peers * CAP
    assigned, position = assignment_slots(expert_ids)
    slot_index = jnp.arange(EXPERTS * CAP, dtype=jnp.int32)
    picker = (slot_index[:, None] == (assigned * CAP + position)[None, :]).astype(jnp.bfloat16)
    picker = picker.reshape(EXPERTS * CAP, tok_count, 2).sum(axis=2)
    packed = jnp.dot(picker, tokens, preferred_element_type=jnp.float32).astype(jnp.bfloat16)
    packed = packed.reshape(EXPERTS, CAP, slice_width)
    n_z, n_x = lax.axis_size(LOOP_AXES[0]), lax.axis_size(LOOP_AXES[1])
    outgoing = jnp.broadcast_to(
        jnp.repeat(packed, halves, axis=0)[:, None], (peers, n_z, CAP, slice_width)
    ).reshape(peers * n_z, CAP, slice_width)
    arrived = lax.all_to_all(
        outgoing, GROUP_AXES + LOOP_AXES[:1], split_axis=0, concat_axis=0, tiled=True
    ).reshape(peers, n_z, CAP, slice_width)
    lane = 128
    planes = arrived.transpose(1, 0, 2, 3).reshape(n_z, rows * slice_width // lane, lane)
    spread = lax.all_to_all(
        jnp.broadcast_to(planes[None], (n_x,) + planes.shape), LOOP_AXES[1], 0, 0, tiled=True
    )
    other = swap_cores(spread)
    segment = jnp.concatenate([spread, other], axis=2).reshape(n_x, n_z, 2 * rows, slice_width)
    by_block = (n_z, n_x, slice_width, hidden_width)
    gate_sum = jnp.einsum(
        "xzrf,zxfh->rh", segment, gate_weight[0].reshape(by_block), preferred_element_type=jnp.float32
    )
    up_sum = jnp.einsum(
        "xzrf,zxfh->rh", segment, up_weight[0].reshape(by_block), preferred_element_type=jnp.float32
    )
    hidden = (jax.nn.silu(gate_sum) * up_sum).astype(jnp.bfloat16)
    down_cols = down_weight[0].reshape(hidden_width, n_z, n_x, slice_width).transpose(0, 2, 1, 3)
    down_cols = down_cols.reshape(hidden_width, model_width)
    own = jnp.dot(hidden[:rows], down_cols, preferred_element_type=jnp.float32)
    partner = swap_cores(
        jnp.dot(hidden[rows:], down_cols, preferred_element_type=jnp.float32).astype(jnp.bfloat16)
    )
    pair = (own + partner.astype(jnp.float32)).astype(jnp.bfloat16)
    by_x = pair.reshape(rows, n_x, n_z * slice_width).transpose(1, 0, 2)
    x_sum = lax.all_to_all(by_x, LOOP_AXES[1], 0, 0, tiled=True)
    x_sum = x_sum.astype(jnp.float32).sum(axis=0).astype(jnp.bfloat16)
    chunks = x_sum.reshape(peers, CAP, n_z, slice_width).transpose(0, 2, 1, 3)
    back = lax.all_to_all(
        chunks.reshape(peers * n_z, CAP, slice_width), GROUP_AXES + LOOP_AXES[:1], 0, 0, tiled=True
    )
    returned = back.reshape(peers, n_z, CAP, slice_width).astype(jnp.float32).sum(axis=1)
    returned = returned.astype(jnp.bfloat16).reshape(rows, slice_width)
    column_index = jnp.arange(rows, dtype=jnp.int32)
    same_expert = (column_index // CAP // halves)[None, :] == assigned[:, None]
    same_slot = (column_index % CAP)[None, :] == position[:, None]
    collector = (same_expert & same_slot).astype(jnp.bfloat16)
    gathered = jnp.dot(collector, returned, preferred_element_type=jnp.float32).reshape(
        tok_count, 2, slice_width
    )
    weights = jax.nn.sigmoid(route_logits - route_logits[:, ::-1])
    mixed = jnp.sum(weights[:, :, None] * gathered, axis=1)
    return mixed.astype(jnp.bfloat16)


def solution(mesh):
    dp, loop = mesh.shape["dp"], mesh.shape["loop"]
    fine = Mesh(
        mesh.devices.reshape(2, dp // 8, 2, 2, loop // 4, 4), GROUP_AXES + ("c",) + LOOP_AXES
    )
    dp_axes = GROUP_AXES + ("c",)
    in_specs = (
        P(dp_axes, LOOP_AXES),
        P(dp_axes, None),
        P(dp_axes, None),
        P(dp_axes, None, LOOP_AXES),
        P(dp_axes, None, LOOP_AXES),
        P(dp_axes, LOOP_AXES, None),
    )
    out_specs = P(dp_axes, LOOP_AXES)
    return jax.shard_map(body, mesh=fine, in_specs=in_specs, out_specs=out_specs, check_vma=False)
```

```python
import jax
import jax.numpy as jnp
from jax import lax
from jax.sharding import Mesh
from jax.sharding import PartitionSpec as P

EXPERTS = 8
CAP = 10
GROUP_AXES = ("zl", "yh", "yl")
LOOP_AXES = ("zh", "x")


def assignment_slots(expert_ids):
    assigned = expert_ids.reshape(-1)
    onehot = (assigned[:, None] == jnp.arange(EXPERTS, dtype=jnp.int32)[None, :]).astype(jnp.int32)
    before = jnp.cumsum(onehot, axis=0) - onehot
    return (assigned, jnp.sum(before * onehot, axis=1))


def swap_cores(x):
    return lax.ppermute(x, "c", [(0, 1), (1, 0)])


def body(tokens, expert_ids, route_logits, gate_weight, up_weight, down_weight):
    peers = lax.axis_size(GROUP_AXES)
    n_loop = lax.axis_size(LOOP_AXES)
    halves = peers // EXPERTS
    tok_count, slice_width = tokens.shape
    model_width = gate_weight.shape[1]
    hidden_width = gate_weight.shape[2]
    rows = peers * CAP
    assigned, position = assignment_slots(expert_ids)
    slot_index = jnp.arange(EXPERTS * CAP, dtype=jnp.int32)
    picker = (slot_index[:, None] == (assigned * CAP + position)[None, :]).astype(jnp.bfloat16)
    picker = picker.reshape(EXPERTS * CAP, tok_count, 2).sum(axis=2)
    packed = jnp.dot(picker, tokens, preferred_element_type=jnp.float32).astype(jnp.bfloat16)
    packed = packed.reshape(EXPERTS, CAP, slice_width)
    n_z, n_x = lax.axis_size(LOOP_AXES[0]), lax.axis_size(LOOP_AXES[1])
    outgoing = jnp.broadcast_to(
        jnp.repeat(packed, halves, axis=0)[:, None], (peers, n_z, CAP, slice_width)
    ).reshape(peers * n_z, CAP, slice_width)
    arrived = lax.all_to_all(
        outgoing, GROUP_AXES + LOOP_AXES[:1], split_axis=0, concat_axis=0, tiled=True
    ).reshape(peers, n_z, CAP, slice_width)
    lane = 128
    planes = arrived.transpose(1, 0, 2, 3).reshape(n_z, rows * slice_width // lane, lane)
    spread = lax.all_to_all(
        jnp.broadcast_to(planes[None], (n_x,) + planes.shape), LOOP_AXES[1], 0, 0, tiled=True
    )
    other = swap_cores(spread)
    segment = jnp.concatenate([spread, other], axis=2).reshape(n_x, n_z, 2 * rows, slice_width)
    by_block = (n_z, n_x, slice_width, hidden_width)
    gate_sum = jnp.einsum(
        "xzrf,zxfh->rh", segment, gate_weight[0].reshape(by_block), preferred_element_type=jnp.float32
    )
    up_sum = jnp.einsum(
        "xzrf,zxfh->rh", segment, up_weight[0].reshape(by_block), preferred_element_type=jnp.float32
    )
    hidden = (jax.nn.silu(gate_sum) * up_sum).astype(jnp.bfloat16)
    own = jnp.dot(hidden[:rows], down_weight[0], preferred_element_type=jnp.float32)
    partner = swap_cores(
        jnp.dot(hidden[rows:], down_weight[0], preferred_element_type=jnp.float32).astype(jnp.bfloat16)
    )
    pair = (own + partner.astype(jnp.float32)).astype(jnp.bfloat16)
    by_x = pair.reshape(rows, n_z, n_x, slice_width).transpose(2, 0, 1, 3)
    by_x = by_x.reshape(n_x, rows, n_z * slice_width)
    x_sum = lax.all_to_all(by_x, LOOP_AXES[1], 0, 0, tiled=True)
    x_sum = x_sum.astype(jnp.float32).sum(axis=0).astype(jnp.bfloat16)
    chunks = x_sum.reshape(peers, CAP, n_z, slice_width).transpose(0, 2, 1, 3)
    back = lax.all_to_all(
        chunks.reshape(peers * n_z, CAP, slice_width), GROUP_AXES + LOOP_AXES[:1], 0, 0, tiled=True
    )
    returned = back.reshape(peers, n_z, CAP, slice_width).astype(jnp.float32).sum(axis=1)
    returned = returned.astype(jnp.bfloat16).reshape(rows, slice_width)
    column_index = jnp.arange(rows, dtype=jnp.int32)
    same_expert = (column_index // CAP // halves)[None, :] == assigned[:, None]
    same_slot = (column_index % CAP)[None, :] == position[:, None]
    collector = (same_expert & same_slot).astype(jnp.bfloat16)
    gathered = jnp.dot(collector, returned, preferred_element_type=jnp.float32).reshape(
        tok_count, 2, slice_width
    )
    weights = jax.nn.sigmoid(route_logits - route_logits[:, ::-1])
    mixed = jnp.sum(weights[:, :, None] * gathered, axis=1)
    return mixed.astype(jnp.bfloat16)


def solution(mesh):
    dp, loop = mesh.shape["dp"], mesh.shape["loop"]
    fine = Mesh(
        mesh.devices.reshape(2, dp // 8, 2, 2, loop // 4, 4), GROUP_AXES + ("c",) + LOOP_AXES
    )
    dp_axes = GROUP_AXES + ("c",)
    in_specs = (
        P(dp_axes, LOOP_AXES),
        P(dp_axes, None),
        P(dp_axes, None),
        P(dp_axes, None, LOOP_AXES),
        P(dp_axes, None, LOOP_AXES),
        P(dp_axes, LOOP_AXES, None),
    )
    out_specs = P(dp_axes, LOOP_AXES)
    return jax.shard_map(body, mesh=fine, in_specs=in_specs, out_specs=out_specs, check_vma=False)
```
